256 devices in a mesh: dp: 32 (over x, y, core), expert: 8 (over z).
Axes of the slice: x: 4, y: 4, z: 8, core: 2. Of those that a mesh axis runs over, the one named last changes fastest.
Arguments:
- tokens: bfloat16 [16384, 1024], P('dp'), may hold values from -6 to 6
- grad_out: bfloat16 [16384, 1024], P('dp'), may hold values from -3 to 3
- region_ids: int32 [16384], P('dp'), may hold values from 0 to 63, as said below
- slot_ids: int32 [16384], P('dp'), may hold values from 0 to 31, as said below
- weight_in: bfloat16 [64, 1024, 4096], P('dp', None, 'expert'), may hold values from -0.25 to 0.25
- weight_out: bfloat16 [64, 4096, 1024], P('dp', 'expert'), may hold values from -0.09375 to 0.09375
Outputs:
- grad_tokens: bfloat16 [16384, 1024], P('dp', 'expert')
- grad_weight_in: bfloat16 [64, 1024, 4096], P('dp', None, 'expert')
- grad_weight_out: bfloat16 [64, 4096, 1024], P('dp', 'expert')
The draws below stay inside these ranges and needn't reach their ends.
Inputs may be any that keep to these rules, and one draw needn't show every extreme that they name: `region_ids`: among the rows of one index of dp, no expert is named more than 32 times, and one expert drawn from the seed is named exactly 32 times on every index of dp. `slot_ids`: among the rows of one index of dp, rows that name the same expert have different slots.
All inputs are finite; a program needn't handle non-finite values.
Results may differ from the reference program's by a relative error of at most 0.017.
Values may be sent and summed in bfloat16 or wider, within the bound.
No kernel may reach another device: no remote copies, remote signals or barrier semaphores. Data moves between devices by JAX's collectives and lax.ppermute only.
A program may use at most 128 MiB of HBM per device.

```python
import jax
import jax.numpy as jnp
from jax import lax

D = 1024
FF = 4096
TOK_DEV = 512
TOKENS = 16384
EXPERTS = 64
CAP = 32
FFB = 512


def routing_pair(key):
    folded = jax.random.fold_in(key, 11)
    key_hot, key_weight, key_blocks = jax.random.split(folded, 3)
    capacity = 4 * TOK_DEV // EXPERTS
    slot_total = EXPERTS * capacity
    hot_expert = jax.random.randint(key_hot, (), 0, EXPERTS, dtype=jnp.int32)
    levels = jax.random.randint(key_weight, (EXPERTS,), 1, 9, dtype=jnp.int32)
    weight = levels * levels
    counter = jnp.arange(slot_total, dtype=jnp.int32)
    expert_of = counter // capacity
    slot_of = counter % capacity
    slot_weight = weight[expert_of]
    is_hot = expert_of == hot_expert
    is_edge = ((expert_of == 0) | (expert_of == EXPERTS - 1)) & (slot_of == 0)
    block_keys = jax.random.split(key_blocks, TOKENS // TOK_DEV)

    def one_block(block_key):
        key_score, key_shuffle = jax.random.split(block_key)
        raw_score = jax.random.randint(key_score, (slot_total,), 0, 2048, dtype=jnp.int32)
        scores = raw_score * slot_weight * slot_total + counter
        scores = jnp.where(is_edge, jnp.int32(2 ** 30) + counter, scores)
        scores = jnp.where(is_hot, jnp.int32(2 ** 30 + 2 ** 29) + counter, scores)
        ignored, chosen = lax.top_k(scores, TOK_DEV)
        shuffle = jax.random.permutation(key_shuffle, TOK_DEV)
        return chosen[shuffle].astype(jnp.int32)
    return jax.vmap(one_block)(block_keys).reshape(TOKENS)


def draw_region_ids(key, part):
    capacity = 4 * TOK_DEV // EXPERTS
    return (routing_pair(key) // capacity).astype(jnp.int32)


def draw_slot_ids(key, part):
    capacity = 4 * TOK_DEV // EXPERTS
    return (routing_pair(key) % capacity).astype(jnp.int32)


def spiked(array, rng, source, target, shards_of, factor):
    owner, partner = [(jnp.arange(array.shape[axis_at]) // (array.shape[axis_at] // shards_of)).reshape([-1 if axis == axis_at else 1 for axis in range(array.ndim)]) for axis_at in (source, target)]
    chosen = jax.random.permutation(rng, shards_of)[partner]
    strong = (owner == chosen) | (owner == (partner + shards_of // 2) % shards_of)
    return jnp.where(strong, factor * array, array)


def block_levels(own_key, extent, pieces, low, largest):
    factor_of, own = 1.0, jax.random.fold_in(own_key, 6)
    for dim, parts in pieces:
        heights = jnp.exp(jax.random.uniform(jax.random.fold_in(own, dim), (parts,), jnp.float32, low / len(pieces), largest / len(pieces)))
        factor_of = factor_of * jnp.repeat(heights, extent[dim] // parts).reshape([-1 if axis == dim else 1 for axis in range(len(extent))])
    return factor_of


def scatter_about(stream_key, extent, scale, most, pieces=(), kind=jnp.bfloat16):
    values = scale * jax.random.normal(stream_key, extent, jnp.float32)
    if pieces:
        values = values * block_levels(stream_key, extent, pieces, -0.22, 0.18)
    return jnp.clip(values, -most, most).astype(kind)


def heavy_noise(own_key, dims, scale, limit, shards, heavy, kind=jnp.bfloat16):
    drawn = scale * jax.random.normal(own_key, dims, jnp.float32)
    if shards:
        drawn = drawn * block_levels(own_key, dims, shards, -0.22, 0.18)
    return jnp.clip(spiked(drawn, jax.random.fold_in(own_key, 3), *heavy), -limit, limit).astype(kind)


def setup_inputs(seed: int = 0) -> dict:
    seeds = jax.random.split(jax.random.key(seed), 7)
    return {
        "tokens": scatter_about(seeds[0], (TOKENS, D), 1.0, 6.0, ((0, 32),)),
        "grad_out": scatter_about(seeds[1], (TOKENS, D), 0.5, 3.0, ((0, 32),)),
        "region_ids": draw_region_ids(jax.random.fold_in(seeds[6], 71), 0),
        "slot_ids": draw_slot_ids(jax.random.fold_in(seeds[6], 71), 0),
        "weight_in": heavy_noise(seeds[4], (EXPERTS, D, FF), D ** -0.5, 0.25, ((0, 32), (2, 8)), (2, 1, 8, 2.0)),
        "weight_out": scatter_about(seeds[5], (EXPERTS, FF, D), FF ** -0.5, 0.09375, ((0, 32), (1, 8))),
    }


def reference(tokens, grad_out, region_ids, slot_ids, weight_in, weight_out):
    slot_rows = (TOKENS // TOK_DEV) * CAP
    block_ids = jnp.arange(TOKENS, dtype=jnp.int32) // TOK_DEV
    position = (block_ids * CAP + slot_ids).astype(jnp.int32)
    routed_in = jnp.zeros((EXPERTS, slot_rows, D), jnp.bfloat16).at[region_ids, position].set(tokens)
    routed_grad = jnp.zeros((EXPERTS, slot_rows, D), jnp.bfloat16).at[region_ids, position].set(grad_out)

    def per_expert(operands):
        expert_in, expert_grad, expert_win, expert_wout = operands
        pre_act = jnp.dot(expert_in, expert_win, preferred_element_type=jnp.float32)
        gate_sig = jax.nn.sigmoid(pre_act)
        hidden_act = (pre_act * gate_sig).astype(jnp.bfloat16)
        back_grad = jnp.dot(expert_grad, expert_wout.T, preferred_element_type=jnp.float32)
        pre_grad = (back_grad * gate_sig * (1.0 + pre_act * (1.0 - gate_sig))).astype(jnp.bfloat16)
        grad_wout = jnp.dot(hidden_act.T, expert_grad, preferred_element_type=jnp.float32).astype(jnp.bfloat16)
        grad_win = jnp.dot(expert_in.T, pre_grad, preferred_element_type=jnp.float32).astype(jnp.bfloat16)
        running = jnp.zeros((slot_rows, D), jnp.float32)
        for hidden_block in range(FF // FFB):
            lower = hidden_block * FFB
            partial_value = jnp.dot(pre_grad[:, lower:lower + FFB], expert_win[:, lower:lower + FFB].T, preferred_element_type=jnp.float32)
            partial_value = lax.optimization_barrier(partial_value.astype(jnp.bfloat16))
            running = running + partial_value.astype(jnp.float32)
        return running.astype(jnp.bfloat16), grad_win, grad_wout

    routed_sum, grad_weight_in, grad_weight_out = lax.map(per_expert, (routed_in, routed_grad, weight_in, weight_out))
    grad_tokens = routed_sum[region_ids, position]
    return grad_tokens, grad_weight_in, grad_weight_out
```

```python
import jax
import jax.numpy as jnp
from jax import lax
from jax.sharding import PartitionSpec as P

CHUNKS = 4


def on_device(tokens, grad_out, region_ids, slot_ids, weight_in, weight_out):
    owners = lax.axis_size("dp")
    local_count = weight_in.shape[0]
    model_width = tokens.shape[1]
    tok_rows = tokens.shape[0]
    experts_all = local_count * owners
    capacity = 4 * tok_rows // experts_all
    step = capacity // CHUNKS
    where_to = region_ids * capacity + slot_ids
    both = jnp.concatenate([tokens, grad_out], axis=1)

    grad_win = None
    grad_wout = None
    back_parts = []
    for chunk in range(CHUNKS):
        rows = jnp.arange(experts_all * step, dtype=jnp.int32)
        expert_of = rows // step
        slot_of = rows % step + chunk * step
        pick = (
            (region_ids[None, :] == expert_of[:, None]) & (slot_ids[None, :] == slot_of[:, None])
        ).astype(jnp.bfloat16)
        sent = jnp.dot(pick, both, preferred_element_type=jnp.float32).astype(jnp.bfloat16)
        sent = sent.reshape(owners, local_count, step, 2, model_width)
        sent = jnp.moveaxis(sent, 3, 1).reshape(owners, 2 * local_count, step, model_width)
        got = lax.all_to_all(sent, "dp", split_axis=0, concat_axis=2, tiled=True)[0]
        routed_in = got[:local_count]
        routed_grad = got[local_count:]
        pre_act = jnp.einsum(
            "erd,edf->erf", routed_in, weight_in, preferred_element_type=jnp.float32
        )
        gate_sig = jax.nn.sigmoid(pre_act)
        hidden_act = (pre_act * gate_sig).astype(jnp.bfloat16)
        back_grad = jnp.einsum(
            "erd,efd->erf", routed_grad, weight_out, preferred_element_type=jnp.float32
        )
        pre_grad = (back_grad * gate_sig * (1.0 + pre_act * (1.0 - gate_sig))).astype(
            jnp.bfloat16
        )
        part_wout = jnp.einsum(
            "erf,erd->efd", hidden_act, routed_grad, preferred_element_type=jnp.float32
        )
        part_win = jnp.einsum(
            "erd,erf->edf", routed_in, pre_grad, preferred_element_type=jnp.float32
        )
        grad_wout = part_wout if grad_wout is None else grad_wout + part_wout
        grad_win = part_win if grad_win is None else grad_win + part_win
        partial_value = jnp.einsum(
            "erf,edf->erd", pre_grad, weight_in, preferred_element_type=jnp.float32
        )
        summed = lax.psum_scatter(
            partial_value.astype(jnp.bfloat16), "expert", scatter_dimension=2, tiled=True
        )
        back_parts.append(
            lax.all_to_all(summed[None], "dp", split_axis=2, concat_axis=0, tiled=True)
        )
    back_rows = jnp.concatenate(back_parts, axis=2)
    grad_tokens = back_rows.reshape(experts_all * capacity, back_rows.shape[3])[where_to]
    return (grad_tokens, grad_win.astype(jnp.bfloat16), grad_wout.astype(jnp.bfloat16))


def solution(mesh):
    in_specs = (
        P("dp", None),
        P("dp", None),
        P("dp"),
        P("dp"),
        P("dp", None, "expert"),
        P("dp", "expert", None),
    )
    out_specs = (P("dp", "expert"), P("dp", None, "expert"), P("dp", "expert", None))
    return jax.shard_map(
        on_device, mesh=mesh, in_specs=in_specs, out_specs=out_specs, check_vma=False
    )
```

```python
import jax
import jax.numpy as jnp
from jax import lax
from jax.sharding import PartitionSpec as P


def on_device(tokens, grad_out, region_ids, slot_ids, weight_in, weight_out):
    owners = lax.axis_size("dp")
    local_count = weight_in.shape[0]
    model_width = tokens.shape[1]
    tok_rows = tokens.shape[0]
    experts_all = local_count * owners
    capacity = 4 * tok_rows // experts_all
    where_to = region_ids * capacity + slot_ids
    both = jnp.concatenate([tokens, grad_out], axis=1)

    rows = jnp.arange(owners * capacity, dtype=jnp.int32)
    owner_of = rows // capacity
    slot_of = rows % capacity
    win_parts, wout_parts, back_parts = [], [], []
    for local in range(local_count):
        expert_of = owner_of * local_count + local
        pick = (
            (region_ids[None, :] == expert_of[:, None]) & (slot_ids[None, :] == slot_of[:, None])
        ).astype(jnp.bfloat16)
        sent = jnp.dot(pick, both, preferred_element_type=jnp.float32).astype(jnp.bfloat16)
        sent = sent.reshape(owners, capacity, 2, model_width)
        got = lax.all_to_all(sent, "dp", split_axis=0, concat_axis=1, tiled=True)[0]
        routed_in = got[:, 0, :]
        routed_grad = got[:, 1, :]
        w_in = weight_in[local]
        w_out = weight_out[local]
        pre_act = jnp.dot(routed_in, w_in, preferred_element_type=jnp.float32)
        gate_sig = jax.nn.sigmoid(pre_act)
        back_grad = lax.dot_general(
            routed_grad, w_out, (((1,), (1,)), ((), ())), preferred_element_type=jnp.float32
        )
        pre_grad = (back_grad * gate_sig * (1.0 + pre_act * (1.0 - gate_sig))).astype(
            jnp.bfloat16
        )
        partial_value = lax.dot_general(
            pre_grad, w_in, (((1,), (1,)), ((), ())), preferred_element_type=jnp.float32
        )
        summed = lax.psum_scatter(
            partial_value.astype(jnp.bfloat16), "expert", scatter_dimension=1, tiled=True
        )
        back_parts.append(
            lax.all_to_all(
                summed.reshape(1, owners, capacity, summed.shape[1]),
                "dp",
                split_axis=1,
                concat_axis=0,
                tiled=True,
            )
        )
        hidden_act = (pre_act * gate_sig).astype(jnp.bfloat16)
        wout_parts.append(
            lax.dot_general(
                hidden_act, routed_grad, (((0,), (0,)), ((), ())),
                preferred_element_type=jnp.float32,
            ).astype(jnp.bfloat16)
        )
        win_parts.append(
            lax.dot_general(
                routed_in, pre_grad, (((0,), (0,)), ((), ())),
                preferred_element_type=jnp.float32,
            ).astype(jnp.bfloat16)
        )
    back_rows = jnp.concatenate(back_parts, axis=1)
    grad_tokens = back_rows.reshape(experts_all * capacity, back_rows.shape[3])[where_to]
    return (grad_tokens, jnp.stack(win_parts), jnp.stack(wout_parts))


def solution(mesh):
    in_specs = (
        P("dp", None),
        P("dp", None),
        P("dp"),
        P("dp"),
        P("dp", None, "expert"),
        P("dp", "expert", None),
    )
    out_specs = (P("dp", "expert"), P("dp", None, "expert"), P("dp", "expert", None))
    return jax.shard_map(
        on_device, mesh=mesh, in_specs=in_specs, out_specs=out_specs, check_vma=False
    )
```

```python
import jax
import jax.numpy as jnp
from jax import lax
from jax.sharding import PartitionSpec as P


def expert_math(routed_in, routed_grad, w_in, w_out):
    pre_act = jnp.dot(routed_in, w_in, preferred_element_type=jnp.float32)
    gate_sig = jax.nn.sigmoid(pre_act)
    back_grad = lax.dot_general(
        routed_grad, w_out, (((1,), (1,)), ((), ())), preferred_element_type=jnp.float32
    )
    pre_grad = (back_grad * gate_sig * (1.0 + pre_act * (1.0 - gate_sig))).astype(jnp.bfloat16)
    partial_value = lax.dot_general(
        pre_grad, w_in, (((1,), (1,)), ((), ())), preferred_element_type=jnp.float32
    ).astype(jnp.bfloat16)
    hidden_act = (pre_act * gate_sig).astype(jnp.bfloat16)
    grad_wout = lax.dot_general(
        hidden_act, routed_grad, (((0,), (0,)), ((), ())), preferred_element_type=jnp.float32
    ).astype(jnp.bfloat16)
    grad_win = lax.dot_general(
        routed_in, pre_grad, (((0,), (0,)), ((), ())), preferred_element_type=jnp.float32
    ).astype(jnp.bfloat16)
    return partial_value, grad_win, grad_wout


def on_device(tokens, grad_out, region_ids, slot_ids, weight_in, weight_out):
    owners = lax.axis_size("dp")
    splits = lax.axis_size("expert")
    local_count = weight_in.shape[0]
    model_width = tokens.shape[1]
    tok_rows = tokens.shape[0]
    experts_all = local_count * owners
    capacity = 4 * tok_rows // experts_all
    where_to = region_ids * capacity + slot_ids
    both = jnp.concatenate([tokens, grad_out], axis=1)
    band = 2 * model_width // splits
    my_band = lax.dynamic_slice_in_dim(both, lax.axis_index("expert") * band, band, axis=1)

    rows = jnp.arange(owners * capacity, dtype=jnp.int32)
    owner_of = rows // capacity
    slot_of = rows % capacity

    def pick_for(local):
        expert_of = owner_of * local_count + local
        return (
            (region_ids[None, :] == expert_of[:, None]) & (slot_ids[None, :] == slot_of[:, None])
        ).astype(jnp.bfloat16)

    sent_b = jnp.dot(pick_for(1), my_band, preferred_element_type=jnp.float32).astype(
        jnp.bfloat16
    )
    got_b = lax.all_to_all(
        sent_b.reshape(owners, capacity, band), "dp", split_axis=0, concat_axis=1, tiled=True
    )[0]
    full_b = lax.all_gather(got_b, "expert", axis=1, tiled=True)
    sent_a = jnp.dot(pick_for(0), both, preferred_element_type=jnp.float32).astype(jnp.bfloat16)
    got_a = lax.all_to_all(
        sent_a.reshape(owners, capacity, 2 * model_width),
        "dp",
        split_axis=0,
        concat_axis=1,
        tiled=True,
    )[0]

    outs = []
    for local, got in ((0, got_a), (1, full_b)):
        outs.append(
            expert_math(
                got[:, :model_width], got[:, model_width:], weight_in[local], weight_out[local]
            )
        )
    partial_value = jnp.stack([o[0] for o in outs])
    summed = lax.psum_scatter(partial_value, "expert", scatter_dimension=2, tiled=True)
    back_rows = lax.all_to_all(
        summed.reshape(1, local_count, owners, capacity, summed.shape[2]),
        "dp",
        split_axis=2,
        concat_axis=0,
        tiled=True,
    )
    grad_tokens = back_rows.reshape(experts_all * capacity, summed.shape[2])[where_to]
    grad_win = jnp.stack([o[1] for o in outs])
    grad_wout = jnp.stack([o[2] for o in outs])
    return (grad_tokens, grad_win, grad_wout)


def solution(mesh):
    in_specs = (
        P("dp", None),
        P("dp", None),
        P("dp"),
        P("dp"),
        P("dp", None, "expert"),
        P("dp", "expert", None),
    )
    out_specs = (P("dp", "expert"), P("dp", None, "expert"), P("dp", "expert", None))
    return jax.shard_map(
        on_device, mesh=mesh, in_specs=in_specs, out_specs=out_specs, check_vma=False
    )
```

```python
import jax
import jax.numpy as jnp
from jax import lax
from jax.experimental.layout import Layout, with_layout_constraint
from jax.sharding import PartitionSpec as P


def expert_math(routed_in, routed_grad, w_in, w_out):
    pre_act = jnp.dot(routed_in, w_in, preferred_element_type=jnp.float32)
    gate_sig = jax.nn.sigmoid(pre_act)
    back_grad = lax.dot_general(
        routed_grad, w_out, (((1,), (1,)), ((), ())), preferred_element_type=jnp.float32
    )
    pre_grad = (back_grad * gate_sig * (1.0 + pre_act * (1.0 - gate_sig))).astype(jnp.bfloat16)
    partial_value = lax.dot_general(
        w_in, pre_grad, (((1,), (1,)), ((), ())), preferred_element_type=jnp.float32
    ).astype(jnp.bfloat16)
    hidden_act = (pre_act * gate_sig).astype(jnp.bfloat16)
    grad_wout = lax.dot_general(
        hidden_act, routed_grad, (((0,), (0,)), ((), ())), preferred_element_type=jnp.float32
    ).astype(jnp.bfloat16)
    grad_win = lax.dot_general(
        routed_in, pre_grad, (((0,), (0,)), ((), ())), preferred_element_type=jnp.float32
    ).astype(jnp.bfloat16)
    return partial_value, grad_win, grad_wout


def on_device(tokens, grad_out, region_ids, slot_ids, weight_in, weight_out):
    owners = lax.axis_size("dp")
    splits = lax.axis_size("expert")
    local_count = weight_in.shape[0]
    model_width = tokens.shape[1]
    tok_rows = tokens.shape[0]
    experts_all = local_count * owners
    capacity = 4 * tok_rows // experts_all
    where_to = region_ids * capacity + slot_ids
    both = jnp.concatenate([tokens, grad_out], axis=1)
    band = 2 * model_width // splits
    my_band = lax.dynamic_slice_in_dim(both, lax.axis_index("expert") * band, band, axis=1)

    rows = jnp.arange(owners * capacity, dtype=jnp.int32)
    owner_of = rows // capacity
    slot_of = rows % capacity

    def pick_for(local):
        expert_of = owner_of * local_count + local
        return (
            (region_ids[None, :] == expert_of[:, None]) & (slot_ids[None, :] == slot_of[:, None])
        ).astype(jnp.bfloat16)

    sent_b = jnp.dot(pick_for(1), my_band, preferred_element_type=jnp.float32).astype(
        jnp.bfloat16
    )
    got_b = lax.all_to_all(
        sent_b.reshape(owners, capacity, band), "dp", split_axis=0, concat_axis=1, tiled=True
    )[0]
    full_b = lax.all_gather(got_b, "expert", axis=1, tiled=True)
    sent_a = jnp.dot(pick_for(0), both, preferred_element_type=jnp.float32).astype(jnp.bfloat16)
    got_a = lax.all_to_all(
        sent_a.reshape(owners, capacity, 2 * model_width),
        "dp",
        split_axis=0,
        concat_axis=1,
        tiled=True,
    )[0]

    outs = []
    for local, got in ((0, got_a), (1, full_b)):
        outs.append(
            expert_math(
                got[:, :model_width], got[:, model_width:], weight_in[local], weight_out[local]
            )
        )
    partial_value = jnp.concatenate([o[0] for o in outs], axis=1)
    partial_value = with_layout_constraint(partial_value, Layout(major_to_minor=(0, 1)))
    summed = lax.psum_scatter(partial_value, "expert", scatter_dimension=0, tiled=True)
    cols = summed.shape[0]
    back_rows = lax.all_to_all(
        summed.reshape(1, cols, local_count, owners, capacity),
        "dp",
        split_axis=3,
        concat_axis=0,
        tiled=True,
    )
    back_rows = jnp.transpose(back_rows[:, :, :, 0, :], (0, 2, 3, 1))
    grad_tokens = back_rows.reshape(experts_all * capacity, cols)[where_to]
    grad_win = jnp.stack([o[1] for o in outs])
    grad_wout = jnp.stack([o[2] for o in outs])
    return (grad_tokens, grad_win, grad_wout)


def solution(mesh):
    in_specs = (
        P("dp", None),
        P("dp", None),
        P("dp"),
        P("dp"),
        P("dp", None, "expert"),
        P("dp", "expert", None),
    )
    out_specs = (P("dp", "expert"), P("dp", None, "expert"), P("dp", "expert", None))
    return jax.shard_map(
        on_device, mesh=mesh, in_specs=in_specs, out_specs=out_specs, check_vma=False
    )
```

```python
import jax
import jax.numpy as jnp
from jax import lax
from jax.experimental.layout import Layout, with_layout_constraint
from jax.sharding import PartitionSpec as P


def expert_math(routed_in, routed_grad, w_in, w_out):
    pre_act = jnp.dot(routed_in, w_in, preferred_element_type=jnp.float32)
    gate_sig = jax.nn.sigmoid(pre_act)
    back_grad = lax.dot_general(
        routed_grad, w_out, (((1,), (1,)), ((), ())), preferred_element_type=jnp.float32
    )
    pre_grad = (back_grad * gate_sig * (1.0 + pre_act * (1.0 - gate_sig))).astype(jnp.bfloat16)
    partial_value = lax.dot_general(
        w_in, pre_grad, (((1,), (1,)), ((), ())), preferred_element_type=jnp.float32
    ).astype(jnp.bfloat16)
    hidden_act = (pre_act * gate_sig).astype(jnp.bfloat16)
    grad_wout = lax.dot_general(
        hidden_act, routed_grad, (((0,), (0,)), ((), ())), preferred_element_type=jnp.float32
    ).astype(jnp.bfloat16)
    grad_win = lax.dot_general(
        routed_in, pre_grad, (((0,), (0,)), ((), ())), preferred_element_type=jnp.float32
    ).astype(jnp.bfloat16)
    return partial_value, grad_win, grad_wout


def ring_reduce_scatter(x, axis):
    n = lax.axis_size(axis)
    me = lax.axis_index(axis)
    blocks = x.reshape(n, x.shape[0] // n, x.shape[1])
    half = x.shape[1] // 2
    fwd = blocks[:, :, :half]
    bwd = blocks[:, :, half:]
    to_next = [(j, (j + 1) % n) for j in range(n)]
    to_prev = [(j, (j - 1) % n) for j in range(n)]

    def block(arr, idx):
        return lax.dynamic_index_in_dim(arr, idx % n, axis=0, keepdims=False)

    acc_f = block(fwd, me - 1)
    acc_b = block(bwd, me + 1)
    for k in range(1, n):
        acc_f = lax.ppermute(acc_f, axis, to_next) + block(fwd, me - 1 - k)
        acc_b = lax.ppermute(acc_b, axis, to_prev) + block(bwd, me + 1 + k)
    return jnp.concatenate([acc_f, acc_b], axis=1)


def on_device(tokens, grad_out, region_ids, slot_ids, weight_in, weight_out):
    owners = lax.axis_size("dp")
    splits = lax.axis_size("expert")
    local_count = weight_in.shape[0]
    model_width = tokens.shape[1]
    tok_rows = tokens.shape[0]
    experts_all = local_count * owners
    capacity = 4 * tok_rows // experts_all
    where_to = region_ids * capacity + slot_ids
    both = jnp.concatenate([tokens, grad_out], axis=1)
    band = 2 * model_width // splits
    my_band = lax.dynamic_slice_in_dim(both, lax.axis_index("expert") * band, band, axis=1)

    rows = jnp.arange(owners * capacity, dtype=jnp.int32)
    owner_of = rows // capacity
    slot_of = rows % capacity

    def pick_for(local):
        expert_of = owner_of * local_count + local
        return (
            (region_ids[None, :] == expert_of[:, None]) & (slot_ids[None, :] == slot_of[:, None])
        ).astype(jnp.bfloat16)

    sent_b = jnp.dot(pick_for(1), my_band, preferred_element_type=jnp.float32).astype(
        jnp.bfloat16
    )
    got_b = lax.all_to_all(
        sent_b.reshape(owners, capacity, band), "dp", split_axis=0, concat_axis=1, tiled=True
    )[0]
    full_b = lax.all_gather(got_b, "expert", axis=1, tiled=True)
    sent_a = jnp.dot(pick_for(0), both, preferred_element_type=jnp.float32).astype(jnp.bfloat16)
    got_a = lax.all_to_all(
        sent_a.reshape(owners, capacity, 2 * model_width),
        "dp",
        split_axis=0,
        concat_axis=1,
        tiled=True,
    )[0]

    outs = []
    for local, got in ((0, got_a), (1, full_b)):
        outs.append(
            expert_math(
                got[:, :model_width], got[:, model_width:], weight_in[local], weight_out[local]
            )
        )
    rows_major = Layout(major_to_minor=(0, 1))
    part_a = with_layout_constraint(outs[0][0], rows_major)
    part_b = with_layout_constraint(outs[1][0], rows_major)
    summed_a = lax.psum_scatter(part_a, "expert", scatter_dimension=0, tiled=True)
    summed_b = ring_reduce_scatter(part_b, "expert")
    summed = jnp.concatenate([summed_a, summed_b], axis=1)
    cols = summed.shape[0]
    back_rows = lax.all_to_all(
        summed.reshape(1, cols, local_count, owners, capacity),
        "dp",
        split_axis=3,
        concat_axis=0,
        tiled=True,
    )
    back_rows = jnp.transpose(back_rows[:, :, :, 0, :], (0, 2, 3, 1))
    grad_tokens = back_rows.reshape(experts_all * capacity, cols)[where_to]
    grad_win = jnp.stack([o[1] for o in outs])
    grad_wout = jnp.stack([o[2] for o in outs])
    return (grad_tokens, grad_win, grad_wout)


def solution(mesh):
    in_specs = (
        P("dp", None),
        P("dp", None),
        P("dp"),
        P("dp"),
        P("dp", None, "expert"),
        P("dp", "expert", None),
    )
    out_specs = (P("dp", "expert"), P("dp", None, "expert"), P("dp", "expert", None))
    return jax.shard_map(
        on_device, mesh=mesh, in_specs=in_specs, out_specs=out_specs, check_vma=False
    )
```

```python
import jax
import jax.numpy as jnp
from jax import lax
from jax.experimental.layout import Layout, with_layout_constraint
from jax.sharding import PartitionSpec as P


def expert_math(routed_in, routed_grad, w_in, w_out):
    pre_act = jnp.dot(routed_in, w_in, preferred_element_type=jnp.float32)
    gate_sig = jax.nn.sigmoid(pre_act)
    back_grad = lax.dot_general(
        routed_grad, w_out, (((1,), (1,)), ((), ())), preferred_element_type=jnp.float32
    )
    pre_grad = (back_grad * gate_sig * (1.0 + pre_act * (1.0 - gate_sig))).astype(jnp.bfloat16)
    partial_value = lax.dot_general(
        w_in, pre_grad, (((1,), (1,)), ((), ())), preferred_element_type=jnp.float32
    ).astype(jnp.bfloat16)
    hidden_act = (pre_act * gate_sig).astype(jnp.bfloat16)
    grad_wout = lax.dot_general(
        hidden_act, routed_grad, (((0,), (0,)), ((), ())), preferred_element_type=jnp.float32
    ).astype(jnp.bfloat16)
    grad_win = lax.dot_general(
        routed_in, pre_grad, (((0,), (0,)), ((), ())), preferred_element_type=jnp.float32
    ).astype(jnp.bfloat16)
    return partial_value, grad_win, grad_wout


def on_device(tokens, grad_out, region_ids, slot_ids, weight_in, weight_out):
    owners = lax.axis_size("dp")
    splits = lax.axis_size("expert")
    local_count = weight_in.shape[0]
    model_width = tokens.shape[1]
    tok_rows = tokens.shape[0]
    experts_all = local_count * owners
    capacity = 4 * tok_rows // experts_all
    where_to = region_ids * capacity + slot_ids
    both = jnp.concatenate([tokens, grad_out], axis=1)
    band = 2 * model_width // splits
    band_at = lax.axis_index("expert") * band
    my_band = jnp.where(
        band_at < model_width,
        lax.dynamic_slice_in_dim(tokens, band_at % model_width, band, axis=1),
        lax.dynamic_slice_in_dim(grad_out, band_at % model_width, band, axis=1),
    )

    rows = jnp.arange(owners * capacity, dtype=jnp.int32)
    owner_of = rows // capacity
    slot_of = rows % capacity

    def pick_for(local):
        expert_of = owner_of * local_count + local
        return (
            (region_ids[None, :] == expert_of[:, None]) & (slot_ids[None, :] == slot_of[:, None])
        ).astype(jnp.bfloat16)

    sent_b = jnp.dot(pick_for(1), my_band, preferred_element_type=jnp.float32).astype(
        jnp.bfloat16
    )
    got_b = lax.all_to_all(
        sent_b.reshape(owners, capacity, band), "dp", split_axis=0, concat_axis=1, tiled=True
    )[0]
    full_b = lax.all_gather(got_b, "expert", axis=1, tiled=True)
    sent_a = jnp.dot(pick_for(0), both, preferred_element_type=jnp.float32).astype(jnp.bfloat16)
    got_a = lax.all_to_all(
        sent_a.reshape(owners, capacity, 2 * model_width),
        "dp",
        split_axis=0,
        concat_axis=1,
        tiled=True,
    )[0]

    outs = []
    for local, got in ((0, got_a), (1, full_b)):
        outs.append(
            expert_math(
                got[:, :model_width], got[:, model_width:], weight_in[local], weight_out[local]
            )
        )
    partial_value = jnp.concatenate([o[0] for o in outs], axis=1)
    partial_value = with_layout_constraint(partial_value, Layout(major_to_minor=(0, 1)))
    summed = lax.psum_scatter(partial_value, "expert", scatter_dimension=0, tiled=True)
    cols = summed.shape[0]
    back_rows = lax.all_to_all(
        summed.reshape(1, cols, local_count, owners, capacity),
        "dp",
        split_axis=3,
        concat_axis=0,
        tiled=True,
    )
    back_rows = jnp.transpose(back_rows[:, :, :, 0, :], (0, 2, 3, 1))
    grad_tokens = back_rows.reshape(experts_all * capacity, cols)[where_to]
    grad_win = jnp.stack([o[1] for o in outs])
    grad_wout = jnp.stack([o[2] for o in outs])
    return (grad_tokens, grad_win, grad_wout)


def solution(mesh):
    in_specs = (
        P("dp", None),
        P("dp", None),
        P("dp"),
        P("dp"),
        P("dp", None, "expert"),
        P("dp", "expert", None),
    )
    out_specs = (P("dp", "expert"), P("dp", None, "expert"), P("dp", "expert", None))
    return jax.shard_map(
        on_device, mesh=mesh, in_specs=in_specs, out_specs=out_specs, check_vma=False
    )
```

```python
import jax
import jax.numpy as jnp
from jax import lax
from jax.experimental.layout import Layout, with_layout_constraint
from jax.sharding import PartitionSpec as P


def expert_math(routed_in, routed_grad, w_in, w_out):
    pre_act = jnp.dot(routed_in, w_in, preferred_element_type=jnp.float32)
    gate_sig = jax.nn.sigmoid(pre_act)
    back_grad = lax.dot_general(
        routed_grad, w_out, (((1,), (1,)), ((), ())), preferred_element_type=jnp.float32
    )
    pre_grad = (back_grad * gate_sig * (1.0 + pre_act * (1.0 - gate_sig))).astype(jnp.bfloat16)
    partial_value = lax.dot_general(
        w_in, pre_grad, (((1,), (1,)), ((), ())), preferred_element_type=jnp.float32
    ).astype(jnp.bfloat16)
    hidden_act = (pre_act * gate_sig).astype(jnp.bfloat16)
    grad_wout = lax.dot_general(
        hidden_act, routed_grad, (((0,), (0,)), ((), ())), preferred_element_type=jnp.float32
    ).astype(jnp.bfloat16)
    grad_win = lax.dot_general(
        routed_in, pre_grad, (((0,), (0,)), ((), ())), preferred_element_type=jnp.float32
    ).astype(jnp.bfloat16)
    return partial_value, grad_win, grad_wout


def on_device(tokens, grad_out, region_ids, slot_ids, weight_in, weight_out):
    owners = lax.axis_size("dp")
    splits = lax.axis_size("expert")
    local_count = weight_in.shape[0]
    model_width = tokens.shape[1]
    tok_rows = tokens.shape[0]
    experts_all = local_count * owners
    capacity = 4 * tok_rows // experts_all
    where_to = region_ids * capacity + slot_ids
    both = jnp.concatenate([tokens, grad_out], axis=1)
    band = 2 * model_width // splits
    band_at = lax.axis_index("expert") * band
    my_band = jnp.where(
        band_at < model_width,
        lax.dynamic_slice_in_dim(tokens, band_at % model_width, band, axis=1),
        lax.dynamic_slice_in_dim(grad_out, band_at % model_width, band, axis=1),
    )

    rows = jnp.arange(owners * capacity, dtype=jnp.int32)
    owner_of = rows // capacity
    slot_of = rows % capacity

    def pick_for(local):
        expert_of = owner_of * local_count + local
        return (
            (region_ids[None, :] == expert_of[:, None]) & (slot_ids[None, :] == slot_of[:, None])
        ).astype(jnp.bfloat16)

    sent_b = jnp.dot(pick_for(1), my_band, preferred_element_type=jnp.float32).astype(
        jnp.bfloat16
    )
    got_b = lax.all_to_all(
        sent_b.reshape(owners, capacity, band), "dp", split_axis=0, concat_axis=1, tiled=True
    )[0]
    full_b = lax.all_gather(got_b, "expert", axis=1, tiled=True)
    sent_a = jnp.dot(pick_for(0), both, preferred_element_type=jnp.float32).astype(jnp.bfloat16)
    got_a = lax.all_to_all(
        sent_a.reshape(owners, capacity, 2 * model_width),
        "dp",
        split_axis=0,
        concat_axis=1,
        tiled=True,
    )[0]

    outs = []
    for local, got in ((0, got_a), (1, full_b)):
        outs.append(
            expert_math(
                got[:, :model_width], got[:, model_width:], weight_in[local], weight_out[local]
            )
        )
    rows_major = Layout(major_to_minor=(0, 1))
    rows_each = outs[0][0].shape[1]
    partial_value = jnp.concatenate([outs[0][0], jnp.zeros_like(outs[1][0])], axis=1)
    partial_value = lax.optimization_barrier(with_layout_constraint(partial_value, rows_major))
    partial_value = lax.dynamic_update_slice_in_dim(partial_value, outs[1][0], rows_each, axis=1)
    partial_value = with_layout_constraint(partial_value, rows_major)
    summed = lax.psum_scatter(partial_value, "expert", scatter_dimension=0, tiled=True)
    cols = summed.shape[0]
    back_rows = lax.all_to_all(
        summed.reshape(1, cols, local_count, owners, capacity),
        "dp",
        split_axis=3,
        concat_axis=0,
        tiled=True,
    )
    back_rows = jnp.transpose(back_rows[:, :, :, 0, :], (0, 2, 3, 1))
    grad_tokens = back_rows.reshape(experts_all * capacity, cols)[where_to]
    grad_win = jnp.stack([o[1] for o in outs])
    grad_wout = jnp.stack([o[2] for o in outs])
    return (grad_tokens, grad_win, grad_wout)


def solution(mesh):
    in_specs = (
        P("dp", None),
        P("dp", None),
        P("dp"),
        P("dp"),
        P("dp", None, "expert"),
        P("dp", "expert", None),
    )
    out_specs = (P("dp", "expert"), P("dp", None, "expert"), P("dp", "expert", None))
    return jax.shard_map(
        on_device, mesh=mesh, in_specs=in_specs, out_specs=out_specs, check_vma=False
    )
```

```python
import jax
import jax.numpy as jnp
from jax import lax
from jax.experimental.layout import Layout, with_layout_constraint
from jax.sharding import PartitionSpec as P


def expert_math(routed_in, routed_grad, w_in, w_out):
    pre_act = jnp.dot(routed_in, w_in, preferred_element_type=jnp.float32)
    gate_sig = jax.nn.sigmoid(pre_act)
    back_grad = lax.dot_general(
        routed_grad, w_out, (((1,), (1,)), ((), ())), preferred_element_type=jnp.float32
    )
    pre_grad = (back_grad * gate_sig * (1.0 + pre_act * (1.0 - gate_sig))).astype(jnp.bfloat16)
    partial_value = lax.dot_general(
        w_in, pre_grad, (((1,), (1,)), ((), ())), preferred_element_type=jnp.float32
    ).astype(jnp.bfloat16)
    hidden_act = (pre_act * gate_sig).astype(jnp.bfloat16)
    grad_wout = lax.dot_general(
        hidden_act, routed_grad, (((0,), (0,)), ((), ())), preferred_element_type=jnp.float32
    ).astype(jnp.bfloat16)
    grad_win = lax.dot_general(
        routed_in, pre_grad, (((0,), (0,)), ((), ())), preferred_element_type=jnp.float32
    ).astype(jnp.bfloat16)
    return partial_value, grad_win, grad_wout


def on_device(tokens, grad_out, region_ids, slot_ids, weight_in, weight_out):
    owners = lax.axis_size("dp")
    splits = lax.axis_size("expert")
    local_count = weight_in.shape[0]
    model_width = tokens.shape[1]
    tok_rows = tokens.shape[0]
    experts_all = local_count * owners
    capacity = 4 * tok_rows // experts_all
    where_to = region_ids * capacity + slot_ids
    both = jnp.concatenate([tokens, grad_out], axis=1)
    band = 2 * model_width // splits
    band_at = lax.axis_index("expert") * band
    my_band = jnp.where(
        band_at < model_width,
        lax.dynamic_slice_in_dim(tokens, band_at % model_width, band, axis=1),
        lax.dynamic_slice_in_dim(grad_out, band_at % model_width, band, axis=1),
    )

    rows = jnp.arange(owners * capacity, dtype=jnp.int32)
    owner_of = rows // capacity
    slot_of = rows % capacity

    def pick_for(local):
        expert_of = owner_of * local_count + local
        return (
            (region_ids[None, :] == expert_of[:, None]) & (slot_ids[None, :] == slot_of[:, None])
        ).astype(jnp.bfloat16)

    sent_b = jnp.dot(pick_for(1), my_band, preferred_element_type=jnp.float32).astype(
        jnp.bfloat16
    )
    got_b = lax.all_to_all(
        sent_b.reshape(owners, capacity, band), "dp", split_axis=0, concat_axis=1, tiled=True
    )[0]
    full_b = lax.all_gather(got_b, "expert", axis=1, tiled=True)
    sent_a = jnp.dot(pick_for(0), both, preferred_element_type=jnp.float32).astype(jnp.bfloat16)
    got_a = lax.all_to_all(
        sent_a.reshape(owners, capacity, 2 * model_width),
        "dp",
        split_axis=0,
        concat_axis=1,
        tiled=True,
    )[0]

    outs = []
    for local, got in ((0, got_a), (1, full_b)):
        outs.append(
            expert_math(
                got[:, :model_width], got[:, model_width:], weight_in[local], weight_out[local]
            )
        )
    partial_value = jnp.concatenate([o[0] for o in outs], axis=1)
    partial_value = with_layout_constraint(partial_value, Layout(major_to_minor=(0, 1)))
    summed = lax.psum_scatter(partial_value, "expert", scatter_dimension=0, tiled=True)
    cols = summed.shape[0]
    back_rows = lax.all_to_all(
        summed.reshape(1, cols, local_count, owners, capacity),
        "dp",
        split_axis=3,
        concat_axis=0,
        tiled=True,
    )
    slots = jnp.arange(experts_all * capacity, dtype=jnp.int32)
    take = (where_to[:, None] == slots[None, :]).astype(jnp.bfloat16)
    take = take.reshape(tok_rows, owners, local_count, capacity)
    grad_tokens = lax.dot_general(
        take, back_rows[:, :, :, 0, :], (((1, 2, 3), (0, 2, 3)), ((), ())),
        preferred_element_type=jnp.float32,
    ).astype(jnp.bfloat16)
    grad_win = jnp.stack([o[1] for o in outs])
    grad_wout = jnp.stack([o[2] for o in outs])
    return (grad_tokens, grad_win, grad_wout)


def solution(mesh):
    in_specs = (
        P("dp", None),
        P("dp", None),
        P("dp"),
        P("dp"),
        P("dp", None, "expert"),
        P("dp", "expert", None),
    )
    out_specs = (P("dp", "expert"), P("dp", None, "expert"), P("dp", "expert", None))
    return jax.shard_map(
        on_device, mesh=mesh, in_specs=in_specs, out_specs=out_specs, check_vma=False
    )
```

```python
import jax
import jax.numpy as jnp
from jax import lax
from jax.experimental.layout import Layout, with_layout_constraint
from jax.sharding import PartitionSpec as P


def expert_math(routed_in, routed_grad, w_in, w_out):
    pre_act = jnp.dot(routed_in, w_in, preferred_element_type=jnp.float32)
    gate_sig = jax.nn.sigmoid(pre_act)
    back_grad = lax.dot_general(
        routed_grad, w_out, (((1,), (1,)), ((), ())), preferred_element_type=jnp.float32
    )
    pre_grad = (back_grad * gate_sig * (1.0 + pre_act * (1.0 - gate_sig))).astype(jnp.bfloat16)
    partial_value = lax.dot_general(
        w_in, pre_grad, (((1,), (1,)), ((), ())), preferred_element_type=jnp.float32
    ).astype(jnp.bfloat16)
    hidden_act = (pre_act * gate_sig).astype(jnp.bfloat16)
    grad_wout = lax.dot_general(
        hidden_act, routed_grad, (((0,), (0,)), ((), ())), preferred_element_type=jnp.float32
    ).astype(jnp.bfloat16)
    grad_win = lax.dot_general(
        routed_in, pre_grad, (((0,), (0,)), ((), ())), preferred_element_type=jnp.float32
    ).astype(jnp.bfloat16)
    return partial_value, grad_win, grad_wout


def on_device(tokens, grad_out, region_ids, slot_ids, weight_in, weight_out):
    owners = lax.axis_size("dp")
    splits = lax.axis_size("expert")
    local_count = weight_in.shape[0]
    model_width = tokens.shape[1]
    tok_rows = tokens.shape[0]
    experts_all = local_count * owners
    capacity = 4 * tok_rows // experts_all
    where_to = region_ids * capacity + slot_ids
    both = jnp.concatenate([tokens, grad_out], axis=1)
    band = 2 * model_width // splits
    band_at = lax.axis_index("expert") * band
    band_tok = lax.dynamic_slice_in_dim(tokens, band_at % model_width, band, axis=1)
    band_grad = lax.dynamic_slice_in_dim(grad_out, band_at % model_width, band, axis=1)

    rows = jnp.arange(owners * capacity, dtype=jnp.int32)
    owner_of = rows // capacity
    slot_of = rows % capacity

    def pick_for(local):
        expert_of = owner_of * local_count + local
        return (
            (region_ids[None, :] == expert_of[:, None]) & (slot_ids[None, :] == slot_of[:, None])
        ).astype(jnp.bfloat16)

    pick_b = pick_for(1)
    sent_b = jnp.where(
        band_at < model_width,
        jnp.dot(pick_b, band_tok, preferred_element_type=jnp.float32),
        jnp.dot(pick_b, band_grad, preferred_element_type=jnp.float32),
    ).astype(jnp.bfloat16)
    got_b = lax.all_to_all(
        sent_b.reshape(owners, capacity, band), "dp", split_axis=0, concat_axis=1, tiled=True
    )[0]
    full_b = lax.all_gather(got_b, "expert", axis=1, tiled=True)
    sent_a = jnp.dot(pick_for(0), both, preferred_element_type=jnp.float32).astype(jnp.bfloat16)
    got_a = lax.all_to_all(
        sent_a.reshape(owners, capacity, 2 * model_width),
        "dp",
        split_axis=0,
        concat_axis=1,
        tiled=True,
    )[0]

    outs = []
    for local, got in ((0, got_a), (1, full_b)):
        outs.append(
            expert_math(
                got[:, :model_width], got[:, model_width:], weight_in[local], weight_out[local]
            )
        )
    partial_value = jnp.concatenate([o[0] for o in outs], axis=1)
    partial_value = with_layout_constraint(partial_value, Layout(major_to_minor=(0, 1)))
    summed = lax.psum_scatter(partial_value, "expert", scatter_dimension=0, tiled=True)
    cols = summed.shape[0]
    back_rows = lax.all_to_all(
        summed.reshape(1, cols, local_count, owners, capacity),
        "dp",
        split_axis=3,
        concat_axis=0,
        tiled=True,
    )
    back_rows = jnp.transpose(back_rows[:, :, :, 0, :], (0, 2, 3, 1))
    grad_tokens = back_rows.reshape(experts_all * capacity, cols)[where_to]
    grad_win = jnp.stack([o[1] for o in outs])
    grad_wout = jnp.stack([o[2] for o in outs])
    return (grad_tokens, grad_win, grad_wout)


def solution(mesh):
    in_specs = (
        P("dp", None),
        P("dp", None),
        P("dp"),
        P("dp"),
        P("dp", None, "expert"),
        P("dp", "expert", None),
    )
    out_specs = (P("dp", "expert"), P("dp", None, "expert"), P("dp", "expert", None))
    return jax.shard_map(
        on_device, mesh=mesh, in_specs=in_specs, out_specs=out_specs, check_vma=False
    )
```
